512 devices in a mesh: ax: 32 (over z, x_hi), pen: 16 (over x_lo, y, core).
Axes of the slice: x: 4 (x_hi: 2, x_lo: 2; x = x_hi * 2 + x_lo), y: 4, z: 16, core: 2. Of those that a mesh axis runs over, the one named last changes fastest.
Arguments:
- fields: float32 [2, 5, 512, 192, 128], P(None, None, 'ax', 'pen'), may hold values from -0.8 to 0.8, as said below
- axial_mean: float32 [512, 192, 128], P('ax', 'pen'), may hold values from 0.2 to 1.5
- radial_mean: float32 [512, 192, 128], P('ax', 'pen'), may hold values from -0.3 to 0.3
- swirl_mean: float32 [512, 192, 128], P('ax', 'pen'), may hold values from -0.3 to 0.3
- density: float32 [512, 192, 128], P('ax', 'pen'), may hold values from 0.5 to 2
- pressure: float32 [512, 192, 128], P('ax', 'pen'), may hold values from 0.4 to 1.2
Outputs:
- residual: float32 [2, 5, 512, 192, 128], P(None, None, 'ax', 'pen')
The draws below stay inside these ranges and needn't reach their ends.
Inputs may be any that keep to these rules, and one draw needn't show every extreme that they name: `fields`: each entry is a draw times (1 - c_j^2)^2 with c_j = cos(pi j / 191) at radial node j, so every field vanishes at both radial ends.
All inputs are finite; a program needn't handle non-finite values.
Results may differ from the reference program's by a relative error of at most 0.0001.
Values sent between devices are 32-bit elements; how exact they have to be, the bound alone decides.
No kernel may reach another device: no remote copies, remote signals or barrier semaphores. Data moves between devices by JAX's collectives and lax.ppermute only.
A program may use at most 64 MiB of HBM per device.

```python
import math
import jax
import jax.numpy as jnp
import numpy as np
from jax import lax

NR = 192
NT = 128
XS = 16
NX = 512
N_AX = 32


def draw_fields(key, part):
    node_index = jnp.arange(NR, dtype=jnp.float32)
    cheb_nodes = jnp.cos(jnp.pi * node_index / (NR - 1))
    radial_weight = ((1.0 - cheb_nodes * cheb_nodes) ** 2)[:, None]
    shape = (2, 5, NX, NR, NT)
    values = 0.2 * jnp.clip(jax.random.normal(key, shape, jnp.float32), -4.0, 4.0)
    return values * radial_weight


def steps_of(own_key, dims, pieces, smallest, top_value):
    loudness, own = 1.0, jax.random.fold_in(own_key, 6)
    for position, shards_of in pieces:
        draws = jnp.exp(jax.random.uniform(jax.random.fold_in(own, position), (shards_of,), jnp.float32, smallest / len(pieces), top_value / len(pieces)))
        loudness = loudness * jnp.repeat(draws, dims[position] // shards_of).reshape([-1 if axis == position else 1 for axis in range(len(dims))])
    return loudness


def setup_inputs(seed: int = 0) -> dict:
    key_list = jax.random.split(jax.random.key(seed), 7)
    return {
        "fields": draw_fields(jax.random.fold_in(key_list[6], 71), 0),
        "axial_mean": jnp.clip(jnp.exp(math.log(1.5) - 2.014903 * jax.random.uniform(key_list[1], (NX, NR, NT), jnp.float32) ** steps_of(key_list[1], (NX, NR, NT), ((0, 32), (1, 16)), -0.2, 0.2)), 0.2, 1.5),
        "radial_mean": jnp.clip(jax.random.uniform(key_list[2], (NX, NR, NT), jnp.float32, -0.3, 0.3) * steps_of(key_list[2], (NX, NR, NT), ((0, 32), (1, 16)), -0.4, 0.0), -0.3, 0.3),
        "swirl_mean": jnp.clip(jax.random.uniform(key_list[3], (NX, NR, NT), jnp.float32, -0.3, 0.3) * steps_of(key_list[3], (NX, NR, NT), ((0, 32), (1, 16)), -0.4, 0.0), -0.3, 0.3),
        "density": jnp.clip(jnp.exp(math.log(2.0) - 1.3862944 * jax.random.uniform(key_list[4], (NX, NR, NT), jnp.float32) ** steps_of(key_list[4], (NX, NR, NT), ((0, 32), (1, 16)), -0.2, 0.2)), 0.5, 2.0),
        "pressure": jnp.clip(jnp.exp(math.log(1.2) - 1.0986123 * jax.random.uniform(key_list[5], (NX, NR, NT), jnp.float32) ** steps_of(key_list[5], (NX, NR, NT), ((0, 32), (1, 16)), -0.2, 0.2)), 0.4, 1.2),
    }


angular_frequency = 1.7
viscosity = 0.01
conduction = 0.014
gamma_ratio = 1.4
spacing = 0.1
radius_inner = 0.5
radius_outer = 6.5
first_axial = (0.8, -0.2, 4.0 / 105.0, -1.0 / 280.0)
axial_second_derivative = (-205.0 / 72.0, 1.6, -0.2, 8.0 / 315.0, -1.0 / 560.0)
highest = lax.Precision.HIGHEST


def cheb_tables(node_count):
    last_node = node_count - 1
    node_index = np.arange(node_count)
    cheb_nodes = np.cos(np.pi * node_index / last_node)
    end_weight = np.where((node_index == 0) | (node_index == last_node), 2.0, 1.0) * np.where(node_index % 2 == 0, 1.0, -1.0)
    row_index = node_index[:, None]
    col_index = node_index[None, :]
    node_gap = -2.0 * np.sin(np.pi * (row_index + col_index) / (2 * last_node)) * np.sin(np.pi * (row_index - col_index) / (2 * last_node))
    off_diag = row_index != col_index
    safe_gap = np.where(off_diag, node_gap, 1.0)
    matrix = np.where(off_diag, end_weight[:, None] / end_weight[None, :] / safe_gap, 0.0)
    row_total = matrix.sum(axis=1)
    matrix = np.where(off_diag, matrix, -row_total[:, None])
    order_first_terms = matrix * (-2.0 / (radius_outer - radius_inner))
    second_order = order_first_terms @ order_first_terms
    radius_nodes = radius_inner + (radius_outer - radius_inner) * (1.0 - cheb_nodes) / 2.0
    return order_first_terms, second_order, radius_nodes


def fourier_tables(point_count):
    offsets = np.arange(point_count)[:, None] - np.arange(point_count)[None, :]
    half_angle = np.pi * offsets / point_count
    sign_table = np.where(offsets % 2 == 0, 1.0, -1.0)
    nonzero = offsets != 0
    safe_sine = np.where(nonzero, np.sin(half_angle), 1.0)
    order_first_terms = np.where(nonzero, 0.5 * sign_table * np.cos(half_angle) / safe_sine, 0.0)
    second_order = np.where(nonzero, -0.5 * sign_table / safe_sine ** 2, -point_count ** 2 / 12.0 - 1.0 / 6.0)
    return order_first_terms, second_order


def build_work(fields, density, pressure):
    thermal_field = fields[:, 4] / density - pressure * fields[:, 3] / (density * density)
    return jnp.concatenate([fields[:, :3], thermal_field[:, None], fields[:, 3:]], axis=1)


def axial_derivatives(padded, planes):
    def shifted(source, offset):
        return lax.slice_in_dim(source, 4 + offset, 4 + offset + planes, axis=2)

    lower = padded[:, :4]
    slope_x = first_axial[0] * (shifted(padded, 1) - shifted(padded, -1))
    curve_x = axial_second_derivative[0] * shifted(lower, 0)
    for offset in range(1, 5):
        if offset > 1:
            slope_x = slope_x + first_axial[offset - 1] * (shifted(padded, offset) - shifted(padded, -offset))
        curve_x = curve_x + axial_second_derivative[offset] * (shifted(lower, offset) + shifted(lower, -offset))
    return slope_x / spacing, curve_x / (spacing * spacing)


def theta_derivatives(work_fields, theta_first, azimuthal_second_derivative):
    slope_t = jnp.dot(work_fields, theta_first, precision=highest)
    curve_t = jnp.dot(work_fields[:, :4], azimuthal_second_derivative, precision=highest)
    return slope_t, curve_t


def radial_derivatives(pencil_block, radial_first, radial_second):
    slope_r = jnp.einsum('sj,abxjt->abxst', radial_first, pencil_block, precision=highest)
    curve_r = jnp.einsum('sj,abxjt->abxst', radial_second, pencil_block[:, :4], precision=highest)
    return slope_r, curve_r


def rotate_phase(value):
    return jnp.stack([-angular_frequency * value[1], angular_frequency * value[0]])


def radial_terms(slope_r, curve_r, radial_mean, density, pressure, inv_radius):
    laplace = curve_r + slope_r[:, :4] * inv_radius
    convect = radial_mean * slope_r
    term_u = convect[:, 0] - viscosity * laplace[:, 0]
    term_v = convect[:, 1] + slope_r[:, 5] / density - viscosity * laplace[:, 1]
    term_w = convect[:, 2] - viscosity * laplace[:, 2]
    term_rho = convect[:, 4] + density * slope_r[:, 1]
    term_p = convect[:, 5] + gamma_ratio * pressure * slope_r[:, 1] - conduction * laplace[:, 3]
    return jnp.stack([term_u, term_v, term_w, term_rho, term_p], axis=1)


def other_terms(work_fields, slope_x, curve_x, slope_t, curve_t, axial_mean, radial_mean, swirl_mean, density, pressure, inv_radius):
    inv_square = inv_radius * inv_radius
    convect = axial_mean * slope_x + swirl_mean * inv_radius * slope_t
    laplace = curve_x + inv_square * curve_t
    vel_u = work_fields[:, 0]
    vel_v = work_fields[:, 1]
    vel_w = work_fields[:, 2]
    div_part = slope_x[:, 0] + inv_radius * (vel_v + slope_t[:, 2])
    term_u = rotate_phase(vel_u) + convect[:, 0] + slope_x[:, 5] / density - viscosity * laplace[:, 0]
    term_v = rotate_phase(vel_v) + convect[:, 1] - 2.0 * swirl_mean * inv_radius * vel_w - viscosity * (laplace[:, 1] - inv_square * (vel_v + 2.0 * slope_t[:, 2]))
    term_w = rotate_phase(vel_w) + convect[:, 2] + inv_radius * slope_t[:, 5] / density + inv_radius * (radial_mean * vel_w + swirl_mean * vel_v) - viscosity * (laplace[:, 2] - inv_square * (vel_w - 2.0 * slope_t[:, 1]))
    term_rho = rotate_phase(work_fields[:, 4]) + convect[:, 4] + density * div_part
    term_p = rotate_phase(work_fields[:, 5]) + convect[:, 5] + gamma_ratio * pressure * div_part - conduction * laplace[:, 3]
    return jnp.stack([term_u, term_v, term_w, term_rho, term_p], axis=1)


def reference(fields, axial_mean, radial_mean, swirl_mean, density, pressure):
    first_np, second_np, radius_np = cheb_tables(NR)
    radial_first = jnp.asarray(first_np, jnp.float32)
    radial_second = jnp.asarray(second_np, jnp.float32)
    inv_radius = jnp.asarray(1.0 / radius_np, jnp.float32)[:, None]
    theta_np, theta_second_np = fourier_tables(NT)
    theta_first = jnp.asarray(theta_np.T, jnp.float32)
    azimuthal_second_derivative = jnp.asarray(theta_second_np.T, jnp.float32)
    fields_pad = jnp.pad(fields, ((0, 0), (0, 0), (4, 4), (0, 0), (0, 0)))
    density_pad = jnp.pad(density, ((4, 4), (0, 0), (0, 0)), constant_values=1.0)
    pressure_pad = jnp.pad(pressure, ((4, 4), (0, 0), (0, 0)))

    def one_block(block_index, result):
        start = (block_index * XS).astype(jnp.int32)
        local_fields = lax.dynamic_slice_in_dim(fields_pad, start, XS + 8, 2)
        local_density = lax.dynamic_slice_in_dim(density_pad, start, XS + 8, 0)
        local_pressure = lax.dynamic_slice_in_dim(pressure_pad, start, XS + 8, 0)
        padded = build_work(local_fields, local_density, local_pressure)
        work_fields = lax.slice_in_dim(padded, 4, 4 + XS, axis=2)
        inner_density = lax.slice_in_dim(local_density, 4, 4 + XS, axis=0)
        inner_pressure = lax.slice_in_dim(local_pressure, 4, 4 + XS, axis=0)
        inner_axial = lax.dynamic_slice_in_dim(axial_mean, start, XS, 0)
        inner_radial = lax.dynamic_slice_in_dim(radial_mean, start, XS, 0)
        inner_swirl = lax.dynamic_slice_in_dim(swirl_mean, start, XS, 0)
        slope_x, curve_x = axial_derivatives(padded, XS)
        slope_t, curve_t = theta_derivatives(work_fields, theta_first, azimuthal_second_derivative)
        slope_r, curve_r = radial_derivatives(work_fields, radial_first, radial_second)
        radial_component = radial_terms(slope_r, curve_r, inner_radial, inner_density, inner_pressure, inv_radius)
        block_out = radial_component + other_terms(work_fields, slope_x, curve_x, slope_t, curve_t, inner_axial, inner_radial, inner_swirl, inner_density, inner_pressure, inv_radius)
        return lax.dynamic_update_slice_in_dim(result, block_out, start, 2)

    result = jnp.zeros(fields.shape, jnp.float32)
    return lax.fori_loop(0, N_AX, one_block, result)
```

```python
import jax
import jax.numpy as jnp
import numpy as np
from jax import lax
from jax.sharding import PartitionSpec as P

angular_frequency = 1.7
viscosity = 0.01
conduction = 0.014
gamma_ratio = 1.4
spacing = 0.1
radius_inner = 0.5
radius_outer = 6.5
first_axial = (0.8, -0.2, 4.0 / 105.0, -1.0 / 280.0)
axial_second_derivative = (-205.0 / 72.0, 1.6, -0.2, 8.0 / 315.0, -1.0 / 560.0)
highest = lax.Precision.HIGHEST


def with_halo(array, sides, width):
    for axis, dim in sides:
        size, length = (lax.axis_size(axis), array.shape[dim])
        up = [(i, (i + 1) % size) for i in range(size - 1)]
        down = [(j, i) for i, j in up]
        last = lax.slice_in_dim(array, length - width, length, axis=dim)
        initial = lax.slice_in_dim(array, 0, width, axis=dim)
        before = lax.ppermute(last, axis, up)
        after = lax.ppermute(initial, axis, down)
        array = jnp.concatenate([before, array, after], axis=dim)
    return array


def cheb_tables(node_count):
    last_node = node_count - 1
    node_index = np.arange(node_count)
    cheb_nodes = np.cos(np.pi * node_index / last_node)
    end_weight = np.where((node_index == 0) | (node_index == last_node), 2.0, 1.0) * np.where(
        node_index % 2 == 0, 1.0, -1.0
    )
    row_index = node_index[:, None]
    col_index = node_index[None, :]
    node_gap = (
        -2.0
        * np.sin(np.pi * (row_index + col_index) / (2 * last_node))
        * np.sin(np.pi * (row_index - col_index) / (2 * last_node))
    )
    off_diag = row_index != col_index
    safe_gap = np.where(off_diag, node_gap, 1.0)
    matrix = np.where(off_diag, end_weight[:, None] / end_weight[None, :] / safe_gap, 0.0)
    row_total = matrix.sum(axis=1)
    matrix = np.where(off_diag, matrix, -row_total[:, None])
    order_first_terms = matrix * (-2.0 / (radius_outer - radius_inner))
    second_order = order_first_terms @ order_first_terms
    radius_nodes = radius_inner + (radius_outer - radius_inner) * (1.0 - cheb_nodes) / 2.0
    return (order_first_terms, second_order, radius_nodes)


def fourier_tables(point_count):
    offsets = np.arange(point_count)[:, None] - np.arange(point_count)[None, :]
    half_angle = np.pi * offsets / point_count
    sign_table = np.where(offsets % 2 == 0, 1.0, -1.0)
    nonzero = offsets != 0
    safe_sine = np.where(nonzero, np.sin(half_angle), 1.0)
    order_first_terms = np.where(nonzero, 0.5 * sign_table * np.cos(half_angle) / safe_sine, 0.0)
    second_order = np.where(
        nonzero, -0.5 * sign_table / safe_sine**2, -(point_count**2) / 12.0 - 1.0 / 6.0
    )
    return (order_first_terms, second_order)


def build_work(fields, density, pressure):
    thermal_field = fields[:, 4] / density - pressure * fields[:, 3] / (density * density)
    return jnp.concatenate([fields[:, :3], thermal_field[:, None], fields[:, 3:]], axis=1)


def axial_derivatives(padded, planes):

    def shifted(source, offset):
        return lax.slice_in_dim(source, 4 + offset, 4 + offset + planes, axis=2)

    lower = padded[:, :4]
    slope_x = first_axial[0] * (shifted(padded, 1) - shifted(padded, -1))
    curve_x = axial_second_derivative[0] * shifted(lower, 0)
    for offset in range(1, 5):
        if offset > 1:
            slope_x = slope_x + first_axial[offset - 1] * (
                shifted(padded, offset) - shifted(padded, -offset)
            )
        curve_x = curve_x + axial_second_derivative[offset] * (
            shifted(lower, offset) + shifted(lower, -offset)
        )
    return (slope_x / spacing, curve_x / (spacing * spacing))


def theta_derivatives(work_fields, theta_first, azimuthal_second_derivative):
    slope_t = jnp.dot(work_fields, theta_first, precision=highest)
    curve_t = jnp.dot(work_fields[:, :4], azimuthal_second_derivative, precision=highest)
    return (slope_t, curve_t)


def radial_derivatives(pencil_block, radial_first, radial_second):
    slope_r = jnp.einsum("sj,abxjt->abxst", radial_first, pencil_block, precision=highest)
    curve_r = jnp.einsum("sj,abxjt->abxst", radial_second, pencil_block[:, :4], precision=highest)
    return (slope_r, curve_r)


def rotate_phase(value):
    return jnp.stack([-angular_frequency * value[1], angular_frequency * value[0]])


def radial_terms(slope_r, curve_r, radial_mean, density, pressure, inv_radius):
    laplace = curve_r + slope_r[:, :4] * inv_radius
    convect = radial_mean * slope_r
    term_u = convect[:, 0] - viscosity * laplace[:, 0]
    term_v = convect[:, 1] + slope_r[:, 5] / density - viscosity * laplace[:, 1]
    term_w = convect[:, 2] - viscosity * laplace[:, 2]
    term_rho = convect[:, 4] + density * slope_r[:, 1]
    term_p = convect[:, 5] + gamma_ratio * pressure * slope_r[:, 1] - conduction * laplace[:, 3]
    return jnp.stack([term_u, term_v, term_w, term_rho, term_p], axis=1)


def other_terms(
    work_fields,
    slope_x,
    curve_x,
    slope_t,
    curve_t,
    axial_mean,
    radial_mean,
    swirl_mean,
    density,
    pressure,
    inv_radius,
):
    inv_square = inv_radius * inv_radius
    convect = axial_mean * slope_x + swirl_mean * inv_radius * slope_t
    laplace = curve_x + inv_square * curve_t
    vel_u = work_fields[:, 0]
    vel_v = work_fields[:, 1]
    vel_w = work_fields[:, 2]
    div_part = slope_x[:, 0] + inv_radius * (vel_v + slope_t[:, 2])
    term_u = (
        rotate_phase(vel_u) + convect[:, 0] + slope_x[:, 5] / density - viscosity * laplace[:, 0]
    )
    term_v = (
        rotate_phase(vel_v)
        + convect[:, 1]
        - 2.0 * swirl_mean * inv_radius * vel_w
        - viscosity * (laplace[:, 1] - inv_square * (vel_v + 2.0 * slope_t[:, 2]))
    )
    term_w = (
        rotate_phase(vel_w)
        + convect[:, 2]
        + inv_radius * slope_t[:, 5] / density
        + inv_radius * (radial_mean * vel_w + swirl_mean * vel_v)
        - viscosity * (laplace[:, 2] - inv_square * (vel_w - 2.0 * slope_t[:, 1]))
    )
    term_rho = rotate_phase(work_fields[:, 4]) + convect[:, 4] + density * div_part
    term_p = (
        rotate_phase(work_fields[:, 5])
        + convect[:, 5]
        + gamma_ratio * pressure * div_part
        - conduction * laplace[:, 3]
    )
    return jnp.stack([term_u, term_v, term_w, term_rho, term_p], axis=1)


def pencil_terms(pencil, radial_first, radial_second, inv_radius):
    raw = pencil[:10].reshape((2, 5) + pencil.shape[1:])
    radial_mean, density, pressure = (pencil[10], pencil[11], pencil[12])
    pencil_work = build_work(raw, density, pressure)
    slope_r, curve_r = radial_derivatives(pencil_work, radial_first, radial_second)
    terms = radial_terms(slope_r, curve_r, radial_mean, density, pressure, inv_radius)
    return terms.reshape((10,) + terms.shape[2:])


def per_device(fields, axial_mean, radial_mean, swirl_mean, density, pressure):
    planes = fields.shape[2]
    shard_rows = fields.shape[3]
    grid_points = fields.shape[4]
    total_rows = shard_rows * lax.axis_size("pen")
    first_np, second_np, radius_np = cheb_tables(total_rows)
    radial_first = jnp.asarray(first_np, jnp.float32)
    radial_second = jnp.asarray(second_np, jnp.float32)
    inv_all = jnp.asarray(1.0 / radius_np, jnp.float32)[:, None]
    inv_local = lax.dynamic_slice_in_dim(inv_all, lax.axis_index("pen") * shard_rows, shard_rows, 0)
    theta_np, theta_second_np = fourier_tables(grid_points)
    theta_first = jnp.asarray(theta_np.T, jnp.float32)
    azimuthal_second_derivative = jnp.asarray(theta_second_np.T, jnp.float32)
    outgoing = jnp.concatenate(
        [
            fields.reshape((10,) + fields.shape[2:]),
            radial_mean[None],
            density[None],
            pressure[None],
        ],
        axis=0,
    )
    pencil = lax.all_to_all(outgoing, "pen", split_axis=1, concat_axis=2, tiled=True)
    radial_pencil = pencil_terms(pencil, radial_first, radial_second, inv_all)
    radial_back = lax.all_to_all(radial_pencil, "pen", split_axis=2, concat_axis=1, tiled=True)
    radial_component = radial_back.reshape(fields.shape)
    work_fields = build_work(fields, density, pressure)
    padded = with_halo(work_fields, (("ax", 2),), 4)
    slope_x, curve_x = axial_derivatives(padded, planes)
    slope_t, curve_t = theta_derivatives(work_fields, theta_first, azimuthal_second_derivative)
    return radial_component + other_terms(
        work_fields,
        slope_x,
        curve_x,
        slope_t,
        curve_t,
        axial_mean,
        radial_mean,
        swirl_mean,
        density,
        pressure,
        inv_local,
    )


def solution(mesh):
    placed = (
        P(None, None, "ax", "pen", None),
        P("ax", "pen", None),
        P("ax", "pen", None),
        P("ax", "pen", None),
        P("ax", "pen", None),
        P("ax", "pen", None),
    )
    return jax.shard_map(
        per_device,
        mesh=mesh,
        in_specs=placed,
        out_specs=P(None, None, "ax", "pen", None),
        check_vma=False,
    )
```
